512 devices in a mesh: bond: 32 (over z, core), row: 16 (over y, x).
Axes of the slice: x: 4, y: 4, z: 16, core: 2. Of those that a mesh axis runs over, the one named last changes fastest.
Arguments:
- left_core: float32 [32, 384, 2, 384], P('bond', 'row'), may hold values from -1 to 2
- right_core: float32 [32, 384, 2, 384], P('bond', 'row'), may hold values from -1 to 2
- gate_angles: float32 [32, 6], P('bond'), may hold values from -3.140625 to 3.140625
- sketch: float32 [768, 384], P('bond'), may hold values from -0.21875 to 0.21875
Outputs:
- next_pair: float32 [32, 768, 768], P('bond', 'row')
The draws below stay inside these ranges and needn't reach their ends.
All inputs are finite; a program needn't handle non-finite values.
Results may differ from the reference program's by a relative error of at most 0.0003.
Values sent between devices are 32-bit elements; how exact they have to be, the bound alone decides.
No kernel may reach another device: no remote copies, remote signals or barrier semaphores. Data moves between devices by JAX's collectives and lax.ppermute only.
A program may use at most 64 MiB of HBM per device.

```python
import math
import jax
import jax.numpy as jnp
import numpy as np
from jax import lax

CHI = 384
ITERS = 2
BONDS = 32


def core_draw(key):
    noise_key, diag_key = jax.random.split(key)
    shape = (BONDS, CHI, 2, CHI)
    noise = jnp.clip(jax.random.normal(noise_key, shape, jnp.float32), -4.0, 4.0)
    diagonal = jax.random.uniform(diag_key, (BONDS, CHI, 2, 1), jnp.float32, 0.7, 1.3)
    identity = (lax.broadcasted_iota(jnp.int32, (CHI, CHI), 0) == lax.broadcasted_iota(jnp.int32, (CHI, CHI), 1)).astype(jnp.float32)
    return diagonal * identity[None, :, None, :] + 0.4 / math.sqrt(CHI) * noise


def draw_left_core(key, part):
    return core_draw(jax.random.fold_in(key, 11))


def draw_right_core(key, part):
    return core_draw(jax.random.fold_in(key, 23))


def shard_levels(key, shape, shards, smallest, largest):
    def one(position, parts):
        draws = jax.random.uniform(jax.random.fold_in(jax.random.fold_in(key, 6), position), (parts,), jnp.float32, smallest / len(shards), largest / len(shards))
        return jnp.repeat(jnp.exp(draws), shape[position] // parts).reshape((-1,) + (1,) * (len(shape) - position - 1))

    gain = one(*shards[0])
    for cut in shards[1:]:
        gain = gain * one(*cut)
    return gain


def scatter_about(rng, dims, deviation, reach, shards=(), kind=jnp.bfloat16):
    values = jax.random.normal(rng, dims, jnp.float32) * deviation
    if len(shards) > 0:
        values = shard_levels(rng, dims, shards, -0.22, 0.18) * values
    return jnp.clip(values, min=-reach, max=reach).astype(kind)


def setup_inputs(seed: int = 0) -> dict:
    keys = jax.random.split(jax.random.key(seed), 5)
    left_core = draw_left_core(jax.random.fold_in(keys[4], 71), 0)
    right_core = draw_right_core(jax.random.fold_in(keys[4], 71), 0)
    gate_angles = jnp.clip(jax.random.uniform(keys[2], (BONDS, 6), jnp.float32, -3.140625, 3.140625), -3.140625, 3.140625)
    sketch = scatter_about(keys[3], (2 * CHI, CHI), (2 * CHI) ** -0.5, 0.21875, ((0, 32),), jnp.float32)
    return dict(left_core=left_core, right_core=right_core, gate_angles=gate_angles, sketch=sketch)


HIGHEST = lax.Precision.HIGHEST
PLANES = ((0, 1), (2, 3), (0, 2), (1, 3), (0, 3), (1, 2))

def rotation(first_axis, second_axis, cosine, sine_value):
    unit = np.eye(4, dtype=np.float32)
    diag_part = np.outer(unit[first_axis], unit[first_axis]) + np.outer(unit[second_axis], unit[second_axis])
    skew_part = np.outer(unit[second_axis], unit[first_axis]) - np.outer(unit[first_axis], unit[second_axis])
    rest_part = np.eye(4, dtype=np.float32) - diag_part
    return jnp.asarray(rest_part) + cosine * jnp.asarray(diag_part) + sine_value * jnp.asarray(skew_part)

def build_gate(angles):
    gate_matrix = jnp.eye(4, dtype=jnp.float32)
    for number, plane in enumerate(PLANES):
        rotated = rotation(plane[0], plane[1], jnp.cos(angles[number]), jnp.sin(angles[number]))
        gate_matrix = jnp.dot(rotated.astype(jnp.float32), gate_matrix.astype(jnp.float32), precision=HIGHEST, preferred_element_type=jnp.float32)
    return gate_matrix

def apply_gate(two_site, gate_matrix):
    width = two_site.shape[1] // 2
    blocks = two_site.reshape(two_site.shape[0] // 2, 2, 2, width)
    mixed_gate = jnp.einsum('pqtu,atuc->apqc', gate_matrix.reshape(2, 2, 2, 2), blocks, precision=HIGHEST)
    return mixed_gate.reshape(two_site.shape)

def orthonormal(sketched):
    gram_matrix = jnp.dot(sketched.T.astype(jnp.float32), sketched.astype(jnp.float32), precision=HIGHEST, preferred_element_type=jnp.float32)
    chol_factor = jnp.linalg.cholesky(gram_matrix)
    return lax.linalg.triangular_solve(chol_factor, sketched, left_side=False, lower=True, transpose_a=True)

def reference(left_core, right_core, gate_angles, sketch):

    def one_bond(inputs):
        left_one, right_one, angles = inputs
        two_site = jnp.dot(left_one.reshape(2 * CHI, CHI).astype(jnp.float32), right_one.reshape(CHI, 2 * CHI).astype(jnp.float32), precision=HIGHEST, preferred_element_type=jnp.float32)
        two_site = apply_gate(two_site, build_gate(angles))
        ortho_basis = orthonormal(jnp.dot(two_site.astype(jnp.float32), sketch.astype(jnp.float32), precision=HIGHEST, preferred_element_type=jnp.float32))
        for repeat in range(ITERS):
            projected = jnp.dot(two_site.T.astype(jnp.float32), ortho_basis.astype(jnp.float32), precision=HIGHEST, preferred_element_type=jnp.float32)
            ortho_basis = orthonormal(jnp.dot(two_site.astype(jnp.float32), projected.astype(jnp.float32), precision=HIGHEST, preferred_element_type=jnp.float32))
        carried = jnp.dot(ortho_basis.T.astype(jnp.float32), two_site.astype(jnp.float32), precision=HIGHEST, preferred_element_type=jnp.float32)
        return (carried, ortho_basis)
    carried, bases = lax.map(one_bond, (left_core, right_core, gate_angles))
    incoming = jnp.concatenate([jnp.zeros((1, CHI, 2 * CHI), jnp.float32), carried[:-1]], 0)

    def finish(inputs):
        came_in, ortho_basis = inputs
        return jnp.dot(came_in.reshape(2 * CHI, CHI).astype(jnp.float32), ortho_basis.reshape(CHI, 2 * CHI).astype(jnp.float32), precision=HIGHEST, preferred_element_type=jnp.float32)
    return lax.map(finish, (incoming, bases))
```

```python
import jax
import jax.numpy as jnp
import numpy as np
from jax import lax
from jax.sharding import PartitionSpec as P

ITERS = 2


HIGHEST = lax.Precision.HIGHEST
PLANES = ((0, 1), (2, 3), (0, 2), (1, 3), (0, 3), (1, 2))


def from_behind(value, axis, steps):
    count = lax.axis_size(axis)
    initial, last = (max(0, -steps), min(count, count - steps))
    return lax.ppermute(value, axis, [(source, source + steps) for source in range(initial, last)])


def rotation(first_axis, second_axis, cosine, sine_value):
    unit = np.eye(4, dtype=np.float32)
    diag_part = np.outer(unit[first_axis], unit[first_axis]) + np.outer(
        unit[second_axis], unit[second_axis]
    )
    skew_part = np.outer(unit[second_axis], unit[first_axis]) - np.outer(
        unit[first_axis], unit[second_axis]
    )
    rest_part = np.eye(4, dtype=np.float32) - diag_part
    return (
        jnp.asarray(rest_part)
        + cosine * jnp.asarray(diag_part)
        + sine_value * jnp.asarray(skew_part)
    )


def build_gate(angles):
    gate_matrix = jnp.eye(4, dtype=jnp.float32)
    for number, plane in enumerate(PLANES):
        rotated = rotation(plane[0], plane[1], jnp.cos(angles[number]), jnp.sin(angles[number]))
        gate_matrix = jnp.dot(
            rotated, gate_matrix, precision=HIGHEST, preferred_element_type=jnp.float32
        )
    return gate_matrix


def apply_gate(two_site, gate_matrix):
    width = two_site.shape[1] // 2
    blocks = two_site.reshape(two_site.shape[0] // 2, 2, 2, width)
    mixed_gate = jnp.einsum(
        "pqtu,atuc->apqc", gate_matrix.reshape(2, 2, 2, 2), blocks, precision=HIGHEST
    )
    return mixed_gate.reshape(two_site.shape)


def matmul(left_side, right_side):
    return jnp.dot(left_side, right_side, precision=HIGHEST, preferred_element_type=jnp.float32)


def inner_rows(left_side, right_side):
    return lax.dot_general(
        left_side,
        right_side,
        (((0,), (0,)), ((), ())),
        precision=HIGHEST,
        preferred_element_type=jnp.float32,
    )


def orthonormal(sketched):
    gram_matrix = inner_rows(sketched, sketched)
    chol_factor = jnp.linalg.cholesky(gram_matrix)
    return lax.linalg.triangular_solve(
        chol_factor, sketched, left_side=False, lower=True, transpose_a=True
    )


def on_device(left_core, right_core, gate_angles, sketch):
    width = left_core.shape[3]
    local_sites = left_core.shape[1]
    local_rows = 2 * local_sites
    both = jnp.stack([left_core[0], right_core[0]], axis=1)
    both = lax.all_gather(both, "row", axis=0, tiled=True)
    sites = both.shape[0]
    left_matrix = both[:, 0].reshape(2 * sites, width)
    right_matrix = both[:, 1].reshape(sites, 2 * width)
    two_site = matmul(left_matrix, right_matrix)
    two_site = apply_gate(two_site, build_gate(gate_angles[0]))
    full_sketch = lax.all_gather(sketch, "bond", axis=0, tiled=True)
    ortho_basis = orthonormal(matmul(two_site, full_sketch))
    for repeat in range(ITERS):
        projected = inner_rows(two_site, ortho_basis)
        ortho_basis = orthonormal(matmul(two_site, projected))
    start = lax.axis_index("row") * local_sites
    my_columns = lax.dynamic_slice_in_dim(ortho_basis, start, local_sites, axis=1)
    carried = inner_rows(my_columns, two_site)
    incoming = from_behind(carried, "bond", 1)
    incoming_matrix = incoming.reshape(local_rows, width)
    next_block = matmul(incoming_matrix, ortho_basis.reshape(sites, 2 * width))
    return next_block[None]


def solution(mesh):
    return jax.shard_map(
        on_device,
        mesh=mesh,
        in_specs=(
            P("bond", "row", None, None),
            P("bond", "row", None, None),
            P("bond", None),
            P("bond", None),
        ),
        out_specs=P("bond", "row", None),
        check_vma=False,
    )
```

```python
import jax
import jax.numpy as jnp
import numpy as np
from jax import lax
from jax.experimental import pallas as pl
from jax.experimental.pallas import tpu as pltpu
from jax.sharding import PartitionSpec as P

ITERS = 2


HIGHEST = lax.Precision.HIGHEST
PLANES = ((0, 1), (2, 3), (0, 2), (1, 3), (0, 3), (1, 2))


def from_behind(value, axis, steps):
    count = lax.axis_size(axis)
    initial, last = (max(0, -steps), min(count, count - steps))
    return lax.ppermute(value, axis, [(source, source + steps) for source in range(initial, last)])


def rotation(first_axis, second_axis, cosine, sine_value):
    unit = np.eye(4, dtype=np.float32)
    diag_part = np.outer(unit[first_axis], unit[first_axis]) + np.outer(
        unit[second_axis], unit[second_axis]
    )
    skew_part = np.outer(unit[second_axis], unit[first_axis]) - np.outer(
        unit[first_axis], unit[second_axis]
    )
    rest_part = np.eye(4, dtype=np.float32) - diag_part
    return (
        jnp.asarray(rest_part)
        + cosine * jnp.asarray(diag_part)
        + sine_value * jnp.asarray(skew_part)
    )


def build_gate(angles):
    gate_matrix = jnp.eye(4, dtype=jnp.float32)
    for number, plane in enumerate(PLANES):
        rotated = rotation(plane[0], plane[1], jnp.cos(angles[number]), jnp.sin(angles[number]))
        gate_matrix = jnp.dot(
            rotated, gate_matrix, precision=HIGHEST, preferred_element_type=jnp.float32
        )
    return gate_matrix


def apply_gate(two_site, gate_matrix):
    width = two_site.shape[1] // 2
    blocks = two_site.reshape(two_site.shape[0] // 2, 2, 2, width)
    mixed_gate = jnp.einsum(
        "pqtu,atuc->apqc", gate_matrix.reshape(2, 2, 2, 2), blocks, precision=HIGHEST
    )
    return mixed_gate.reshape(two_site.shape)


def matmul(left_side, right_side):
    return jnp.dot(left_side, right_side, precision=HIGHEST, preferred_element_type=jnp.float32)


def inner_rows(left_side, right_side):
    return lax.dot_general(
        left_side,
        right_side,
        (((0,), (0,)), ((), ())),
        precision=HIGHEST,
        preferred_element_type=jnp.float32,
    )


def pick_row(ref, base, offset, lanes):
    tile = ref[pl.ds(base, 8), lanes]
    sub = lax.broadcasted_iota(jnp.int32, tile.shape, 0)
    return jnp.sum(jnp.where(sub == offset, tile, 0.0), axis=0, keepdims=True)


def chol_inv_kernel(a_ref, w_ref, s_ref):
    n = a_ref.shape[0]
    s_ref[...] = a_ref[...]
    rows = lax.broadcasted_iota(jnp.int32, (n, n), 0)
    cols = lax.broadcasted_iota(jnp.int32, (n, n), 1)
    w_ref[...] = jnp.where(rows == cols, 1.0, 0.0).astype(jnp.float32)
    for q in range(n // 128):
        r0 = q * 128
        m = n - r0
        wl = r0 + 128

        def step(j, carry):
            base = pl.multiple_of((j // 8) * 8, 8)
            offset = j - base
            srow = pick_row(s_ref, base, offset, slice(r0, n))
            lane = lax.broadcasted_iota(jnp.int32, (1, m), 1) + r0
            d = jnp.sum(jnp.where(lane == j, srow, 0.0), axis=1, keepdims=True)
            r = lax.rsqrt(d)
            v_s = jnp.where(lane > j, srow * r, 0.0)
            v_w = pick_row(w_ref, base, offset, slice(0, wl)) * r
            scol = s_ref[r0:n, r0:r0 + 128]
            lane_c = lax.broadcasted_iota(jnp.int32, (m, 128), 1) + r0
            col = jnp.sum(jnp.where(lane_c == j, scol, 0.0), axis=1, keepdims=True)
            row_id = lax.broadcasted_iota(jnp.int32, (m, 1), 0) + r0
            l_col = jnp.where(row_id > j, col * r, 0.0)
            s_ref[r0:n, r0:n] = s_ref[r0:n, r0:n] - l_col * v_s
            w_ref[r0:n, 0:wl] = w_ref[r0:n, 0:wl] - l_col * v_w
            tile = w_ref[pl.ds(base, 8), 0:wl]
            sub = lax.broadcasted_iota(jnp.int32, tile.shape, 0)
            w_ref[pl.ds(base, 8), 0:wl] = jnp.where(sub == offset, v_w, tile)
            return carry

        lax.fori_loop(r0, r0 + 128, step, 0)


def chol_inv(gram):
    n = gram.shape[0]
    return pl.pallas_call(
        chol_inv_kernel,
        out_shape=jax.ShapeDtypeStruct((n, n), jnp.float32),
        in_specs=[pl.BlockSpec(memory_space=pltpu.VMEM)],
        out_specs=pl.BlockSpec(memory_space=pltpu.VMEM),
        scratch_shapes=[pltpu.VMEM((n, n), jnp.float32)],
    )(gram)


def orthonormal(sketched):
    gram_matrix = inner_rows(sketched, sketched)
    gram_matrix = 0.5 * (gram_matrix + gram_matrix.T)
    inverse_factor = chol_inv(gram_matrix)
    return lax.dot_general(
        sketched,
        inverse_factor,
        (((1,), (1,)), ((), ())),
        precision=HIGHEST,
        preferred_element_type=jnp.float32,
    )


def on_device(left_core, right_core, gate_angles, sketch):
    width = left_core.shape[3]
    local_sites = left_core.shape[1]
    local_rows = 2 * local_sites
    both = jnp.stack([left_core[0], right_core[0]], axis=1)
    both = lax.all_gather(both, "row", axis=0, tiled=True)
    sites = both.shape[0]
    left_matrix = both[:, 0].reshape(2 * sites, width)
    right_matrix = both[:, 1].reshape(sites, 2 * width)
    two_site = matmul(left_matrix, right_matrix)
    two_site = apply_gate(two_site, build_gate(gate_angles[0]))
    full_sketch = lax.all_gather(sketch, "bond", axis=0, tiled=True)
    ortho_basis = orthonormal(matmul(two_site, full_sketch))
    for repeat in range(ITERS):
        projected = inner_rows(two_site, ortho_basis)
        ortho_basis = orthonormal(matmul(two_site, projected))
    start = lax.axis_index("row") * local_sites
    my_columns = lax.dynamic_slice_in_dim(ortho_basis, start, local_sites, axis=1)
    carried = inner_rows(my_columns, two_site)
    incoming = from_behind(carried, "bond", 1)
    incoming_matrix = incoming.reshape(local_rows, width)
    next_block = matmul(incoming_matrix, ortho_basis.reshape(sites, 2 * width))
    return next_block[None]


def solution(mesh):
    return jax.shard_map(
        on_device,
        mesh=mesh,
        in_specs=(
            P("bond", "row", None, None),
            P("bond", "row", None, None),
            P("bond", None),
            P("bond", None),
        ),
        out_specs=P("bond", "row", None),
        check_vma=False,
    )
```

```python
import jax
import jax.numpy as jnp
import numpy as np
from jax import lax
from jax.experimental import pallas as pl
from jax.experimental.pallas import tpu as pltpu
from jax.sharding import PartitionSpec as P

ITERS = 2


HIGHEST = lax.Precision.HIGHEST
PLANES = ((0, 1), (2, 3), (0, 2), (1, 3), (0, 3), (1, 2))


def from_behind(value, axis, steps):
    count = lax.axis_size(axis)
    initial, last = (max(0, -steps), min(count, count - steps))
    return lax.ppermute(value, axis, [(source, source + steps) for source in range(initial, last)])


def rotation(first_axis, second_axis, cosine, sine_value):
    unit = np.eye(4, dtype=np.float32)
    diag_part = np.outer(unit[first_axis], unit[first_axis]) + np.outer(
        unit[second_axis], unit[second_axis]
    )
    skew_part = np.outer(unit[second_axis], unit[first_axis]) - np.outer(
        unit[first_axis], unit[second_axis]
    )
    rest_part = np.eye(4, dtype=np.float32) - diag_part
    return (
        jnp.asarray(rest_part)
        + cosine * jnp.asarray(diag_part)
        + sine_value * jnp.asarray(skew_part)
    )


def build_gate(angles):
    gate_matrix = jnp.eye(4, dtype=jnp.float32)
    for number, plane in enumerate(PLANES):
        rotated = rotation(plane[0], plane[1], jnp.cos(angles[number]), jnp.sin(angles[number]))
        gate_matrix = jnp.dot(
            rotated, gate_matrix, precision=HIGHEST, preferred_element_type=jnp.float32
        )
    return gate_matrix


def apply_gate(two_site, gate_matrix):
    width = two_site.shape[1] // 2
    blocks = two_site.reshape(two_site.shape[0] // 2, 2, 2, width)
    mixed_gate = jnp.einsum(
        "pqtu,atuc->apqc", gate_matrix.reshape(2, 2, 2, 2), blocks, precision=HIGHEST
    )
    return mixed_gate.reshape(two_site.shape)


def matmul(left_side, right_side):
    return jnp.dot(left_side, right_side, precision=HIGHEST, preferred_element_type=jnp.float32)


def inner_rows(left_side, right_side):
    return lax.dot_general(
        left_side,
        right_side,
        (((0,), (0,)), ((), ())),
        precision=HIGHEST,
        preferred_element_type=jnp.float32,
    )


def pick_row(ref, base, offset, lanes):
    tile = ref[pl.ds(base, 8), lanes]
    sub = lax.broadcasted_iota(jnp.int32, tile.shape, 0)
    return jnp.sum(jnp.where(sub == offset, tile, 0.0), axis=0, keepdims=True)


def chol_inv_kernel(a_ref, w_ref, s_ref):
    n = a_ref.shape[0]
    s_ref[...] = a_ref[...]
    rows = lax.broadcasted_iota(jnp.int32, (n, n), 0)
    cols = lax.broadcasted_iota(jnp.int32, (n, n), 1)
    w_ref[...] = jnp.where(rows == cols, 1.0, 0.0).astype(jnp.float32)
    for q in range(n // 128):
        r0 = q * 128
        m = n - r0
        wl = r0 + 128

        def step(j, carry):
            base = pl.multiple_of((j // 8) * 8, 8)
            offset = j - base
            srow = pick_row(s_ref, base, offset, slice(r0, n))
            lane = lax.broadcasted_iota(jnp.int32, (1, m), 1) + r0
            d = jnp.sum(jnp.where(lane == j, srow, 0.0), axis=1, keepdims=True)
            r = lax.rsqrt(d)
            v_s = jnp.where(lane > j, srow * r, 0.0)
            v_w = pick_row(w_ref, base, offset, slice(0, wl)) * r
            scol = s_ref[r0:n, r0:r0 + 128]
            lane_c = lax.broadcasted_iota(jnp.int32, (m, 128), 1) + r0
            col = jnp.sum(jnp.where(lane_c == j, scol, 0.0), axis=1, keepdims=True)
            row_id = lax.broadcasted_iota(jnp.int32, (m, 1), 0) + r0
            l_col = jnp.where(row_id > j, col * r, 0.0)
            s_ref[r0:n, r0:n] = s_ref[r0:n, r0:n] - l_col * v_s
            w_ref[r0:n, 0:wl] = w_ref[r0:n, 0:wl] - l_col * v_w
            tile = w_ref[pl.ds(base, 8), 0:wl]
            sub = lax.broadcasted_iota(jnp.int32, tile.shape, 0)
            w_ref[pl.ds(base, 8), 0:wl] = jnp.where(sub == offset, v_w, tile)
            return carry

        lax.fori_loop(r0, r0 + 128, step, 0)


def chol_inv(gram):
    n = gram.shape[0]
    return pl.pallas_call(
        chol_inv_kernel,
        out_shape=jax.ShapeDtypeStruct((n, n), jnp.float32),
        in_specs=[pl.BlockSpec(memory_space=pltpu.VMEM)],
        out_specs=pl.BlockSpec(memory_space=pltpu.VMEM),
        scratch_shapes=[pltpu.VMEM((n, n), jnp.float32)],
    )(gram)


def orthonormal(sketched):
    gram_matrix = inner_rows(sketched, sketched)
    gram_matrix = 0.5 * (gram_matrix + gram_matrix.T)
    inverse_factor = chol_inv(gram_matrix)
    return lax.dot_general(
        sketched,
        inverse_factor,
        (((1,), (1,)), ((), ())),
        precision=HIGHEST,
        preferred_element_type=jnp.float32,
    )


def doubling_gather(block, axis):
    count = lax.axis_size(axis)
    index = lax.axis_index(axis)
    bits = count.bit_length() - 1
    gathered = block[None]
    for bit in reversed(range(bits)):
        mask = 1 << bit
        received = lax.ppermute(gathered, axis, [(source, source ^ mask) for source in range(count)])
        upper = (index & mask) != 0
        gathered = jnp.where(
            upper,
            jnp.stack([received, gathered]),
            jnp.stack([gathered, received]),
        )
    order = tuple(range(bits - 1, -1, -1)) + tuple(range(bits, gathered.ndim))
    gathered = jnp.transpose(gathered, order)
    return gathered.reshape((count * block.shape[0],) + block.shape[1:])


def on_device(left_core, right_core, gate_angles, sketch):
    width = left_core.shape[3]
    local_sites = left_core.shape[1]
    local_rows = 2 * local_sites
    both = jnp.stack([left_core[0], right_core[0]], axis=1)
    both = lax.all_gather(both, "row", axis=0, tiled=True)
    sites = both.shape[0]
    left_matrix = both[:, 0].reshape(2 * sites, width)
    right_matrix = both[:, 1].reshape(sites, 2 * width)
    two_site = matmul(left_matrix, right_matrix)
    two_site = apply_gate(two_site, build_gate(gate_angles[0]))
    full_sketch = doubling_gather(sketch, "bond")
    ortho_basis = orthonormal(matmul(two_site, full_sketch))
    for repeat in range(ITERS):
        projected = inner_rows(two_site, ortho_basis)
        ortho_basis = orthonormal(matmul(two_site, projected))
    start = lax.axis_index("row") * local_sites
    my_columns = lax.dynamic_slice_in_dim(ortho_basis, start, local_sites, axis=1)
    carried = inner_rows(my_columns, two_site)
    incoming = from_behind(carried, "bond", 1)
    incoming_matrix = incoming.reshape(local_rows, width)
    next_block = matmul(incoming_matrix, ortho_basis.reshape(sites, 2 * width))
    return next_block[None]


def solution(mesh):
    return jax.shard_map(
        on_device,
        mesh=mesh,
        in_specs=(
            P("bond", "row", None, None),
            P("bond", "row", None, None),
            P("bond", None),
            P("bond", None),
        ),
        out_specs=P("bond", "row", None),
        check_vma=False,
    )
```

```python
import jax
import jax.numpy as jnp
import numpy as np
from jax import lax
from jax.experimental import pallas as pl
from jax.experimental.pallas import tpu as pltpu
from jax.sharding import PartitionSpec as P

ITERS = 2


HIGHEST = lax.Precision.HIGHEST
PLANES = ((0, 1), (2, 3), (0, 2), (1, 3), (0, 3), (1, 2))


def from_behind(value, axis, steps):
    count = lax.axis_size(axis)
    initial, last = (max(0, -steps), min(count, count - steps))
    return lax.ppermute(value, axis, [(source, source + steps) for source in range(initial, last)])


def rotation(first_axis, second_axis, cosine, sine_value):
    unit = np.eye(4, dtype=np.float32)
    diag_part = np.outer(unit[first_axis], unit[first_axis]) + np.outer(
        unit[second_axis], unit[second_axis]
    )
    skew_part = np.outer(unit[second_axis], unit[first_axis]) - np.outer(
        unit[first_axis], unit[second_axis]
    )
    rest_part = np.eye(4, dtype=np.float32) - diag_part
    return (
        jnp.asarray(rest_part)
        + cosine * jnp.asarray(diag_part)
        + sine_value * jnp.asarray(skew_part)
    )


def build_gate(angles):
    gate_matrix = jnp.eye(4, dtype=jnp.float32)
    for number, plane in enumerate(PLANES):
        rotated = rotation(plane[0], plane[1], jnp.cos(angles[number]), jnp.sin(angles[number]))
        gate_matrix = jnp.dot(
            rotated, gate_matrix, precision=HIGHEST, preferred_element_type=jnp.float32
        )
    return gate_matrix


def apply_gate(two_site, gate_matrix):
    width = two_site.shape[1] // 2
    blocks = two_site.reshape(two_site.shape[0] // 2, 2, 2, width)
    mixed_gate = jnp.einsum(
        "pqtu,atuc->apqc", gate_matrix.reshape(2, 2, 2, 2), blocks, precision=HIGHEST
    )
    return mixed_gate.reshape(two_site.shape)


def matmul(left_side, right_side):
    return jnp.dot(left_side, right_side, precision=HIGHEST, preferred_element_type=jnp.float32)


def inner_rows(left_side, right_side):
    return lax.dot_general(
        left_side,
        right_side,
        (((0,), (0,)), ((), ())),
        precision=HIGHEST,
        preferred_element_type=jnp.float32,
    )


BLOCK = 128


def pick_row(ref, base, offset, lanes):
    tile = ref[pl.ds(base, 8), lanes]
    sub = lax.broadcasted_iota(jnp.int32, tile.shape, 0)
    return jnp.sum(jnp.where(sub == offset, tile, 0.0), axis=0, keepdims=True)


def block_dot(left_side, right_side):
    return jnp.dot(left_side, right_side, precision=HIGHEST, preferred_element_type=jnp.float32)


def chol_inv_kernel(a_ref, w_ref, s_ref):
    n = a_ref.shape[0]
    nb = BLOCK
    blocks = n // nb
    s_ref[...] = a_ref[...]
    w_ref[...] = jnp.zeros((n, n), jnp.float32)
    eye_rows = lax.broadcasted_iota(jnp.int32, (nb, nb), 0)
    eye_cols = lax.broadcasted_iota(jnp.int32, (nb, nb), 1)
    eye = jnp.where(eye_rows == eye_cols, 1.0, 0.0).astype(jnp.float32)
    for p in range(blocks):
        r0 = p * nb
        m = n - r0
        w_ref[r0:r0 + nb, r0:r0 + nb] = eye

        def step(j, carry):
            base = pl.multiple_of((j // 8) * 8, 8)
            offset = j - base
            srow = pick_row(s_ref, base, offset, slice(r0, r0 + nb))
            lane = lax.broadcasted_iota(jnp.int32, (1, nb), 1) + r0
            d = jnp.sum(jnp.where(lane == j, srow, 0.0), axis=1, keepdims=True)
            r = lax.rsqrt(d)
            l_row = jnp.where(lane > j, srow * r, 0.0)
            panel = s_ref[r0:n, r0:r0 + nb]
            lane_p = lax.broadcasted_iota(jnp.int32, (m, nb), 1) + r0
            col = jnp.sum(jnp.where(lane_p == j, panel, 0.0), axis=1, keepdims=True)
            row_id = lax.broadcasted_iota(jnp.int32, (m, 1), 0) + r0
            scaled = col * r
            l_col = jnp.where(row_id > j, scaled, 0.0)
            l_keep = jnp.where(row_id >= j, scaled, 0.0)
            s_ref[r0:n, r0:r0 + nb] = jnp.where(lane_p == j, l_keep, panel - l_col * l_row)
            w_row = pick_row(w_ref, base, offset, slice(r0, r0 + nb)) * r
            w_block = w_ref[r0:r0 + nb, r0:r0 + nb]
            sub = lax.broadcasted_iota(jnp.int32, (nb, nb), 0) + r0
            w_block = jnp.where(sub == j, w_row, w_block - l_col[:nb] * w_row)
            w_ref[r0:r0 + nb, r0:r0 + nb] = w_block
            return carry

        lax.fori_loop(r0, r0 + nb, step, 0)
        if p + 1 < blocks:
            below = s_ref[r0 + nb:n, r0:r0 + nb]
            s_ref[r0 + nb:n, r0 + nb:n] = s_ref[r0 + nb:n, r0 + nb:n] - lax.dot_general(
                below, below, (((1,), (1,)), ((), ())),
                precision=HIGHEST, preferred_element_type=jnp.float32,
            )
    for a in range(1, blocks):
        for b in range(a - 1, -1, -1):
            acc = jnp.zeros((nb, nb), jnp.float32)
            for k in range(b, a):
                acc = acc + block_dot(
                    s_ref[a * nb:(a + 1) * nb, k * nb:(k + 1) * nb],
                    w_ref[k * nb:(k + 1) * nb, b * nb:(b + 1) * nb],
                )
            w_ref[a * nb:(a + 1) * nb, b * nb:(b + 1) * nb] = -block_dot(
                w_ref[a * nb:(a + 1) * nb, a * nb:(a + 1) * nb], acc
            )


def chol_inv(gram):
    n = gram.shape[0]
    return pl.pallas_call(
        chol_inv_kernel,
        out_shape=jax.ShapeDtypeStruct((n, n), jnp.float32),
        in_specs=[pl.BlockSpec(memory_space=pltpu.VMEM)],
        out_specs=pl.BlockSpec(memory_space=pltpu.VMEM),
        scratch_shapes=[pltpu.VMEM((n, n), jnp.float32)],
    )(gram)

def orthonormal(sketched):
    gram_matrix = inner_rows(sketched, sketched)
    gram_matrix = 0.5 * (gram_matrix + gram_matrix.T)
    inverse_factor = chol_inv(gram_matrix)
    return lax.dot_general(
        sketched,
        inverse_factor,
        (((1,), (1,)), ((), ())),
        precision=HIGHEST,
        preferred_element_type=jnp.float32,
    )


def doubling_gather(block, axis):
    count = lax.axis_size(axis)
    index = lax.axis_index(axis)
    bits = count.bit_length() - 1
    gathered = block[None]
    for bit in reversed(range(bits)):
        mask = 1 << bit
        received = lax.ppermute(gathered, axis, [(source, source ^ mask) for source in range(count)])
        upper = (index & mask) != 0
        gathered = jnp.where(
            upper,
            jnp.stack([received, gathered]),
            jnp.stack([gathered, received]),
        )
    order = tuple(range(bits - 1, -1, -1)) + tuple(range(bits, gathered.ndim))
    gathered = jnp.transpose(gathered, order)
    return gathered.reshape((count * block.shape[0],) + block.shape[1:])


def on_device(left_core, right_core, gate_angles, sketch):
    width = left_core.shape[3]
    local_sites = left_core.shape[1]
    local_rows = 2 * local_sites
    both = jnp.stack([left_core[0], right_core[0]], axis=1)
    both = lax.all_gather(both, "row", axis=0, tiled=True)
    sites = both.shape[0]
    left_matrix = both[:, 0].reshape(2 * sites, width)
    right_matrix = both[:, 1].reshape(sites, 2 * width)
    two_site = matmul(left_matrix, right_matrix)
    two_site = apply_gate(two_site, build_gate(gate_angles[0]))
    full_sketch = doubling_gather(sketch, "bond")
    ortho_basis = orthonormal(matmul(two_site, full_sketch))
    for repeat in range(ITERS):
        projected = inner_rows(two_site, ortho_basis)
        ortho_basis = orthonormal(matmul(two_site, projected))
    start = lax.axis_index("row") * local_sites
    my_columns = lax.dynamic_slice_in_dim(ortho_basis, start, local_sites, axis=1)
    carried = inner_rows(my_columns, two_site)
    incoming = from_behind(carried, "bond", 1)
    incoming_matrix = incoming.reshape(local_rows, width)
    next_block = matmul(incoming_matrix, ortho_basis.reshape(sites, 2 * width))
    return next_block[None]


def solution(mesh):
    return jax.shard_map(
        on_device,
        mesh=mesh,
        in_specs=(
            P("bond", "row", None, None),
            P("bond", "row", None, None),
            P("bond", None),
            P("bond", None),
        ),
        out_specs=P("bond", "row", None),
        check_vma=False,
    )
```

```python
import jax
import jax.numpy as jnp
import numpy as np
from jax import lax
from jax.experimental import pallas as pl
from jax.experimental.pallas import tpu as pltpu
from jax.sharding import PartitionSpec as P

ITERS = 2


HIGHEST = lax.Precision.HIGHEST
PLANES = ((0, 1), (2, 3), (0, 2), (1, 3), (0, 3), (1, 2))


def from_behind(value, axis, steps):
    count = lax.axis_size(axis)
    initial, last = (max(0, -steps), min(count, count - steps))
    return lax.ppermute(value, axis, [(source, source + steps) for source in range(initial, last)])


def rotation(first_axis, second_axis, cosine, sine_value):
    unit = np.eye(4, dtype=np.float32)
    diag_part = np.outer(unit[first_axis], unit[first_axis]) + np.outer(
        unit[second_axis], unit[second_axis]
    )
    skew_part = np.outer(unit[second_axis], unit[first_axis]) - np.outer(
        unit[first_axis], unit[second_axis]
    )
    rest_part = np.eye(4, dtype=np.float32) - diag_part
    return (
        jnp.asarray(rest_part)
        + cosine * jnp.asarray(diag_part)
        + sine_value * jnp.asarray(skew_part)
    )


def build_gate(angles):
    gate_matrix = jnp.eye(4, dtype=jnp.float32)
    for number, plane in enumerate(PLANES):
        rotated = rotation(plane[0], plane[1], jnp.cos(angles[number]), jnp.sin(angles[number]))
        gate_matrix = jnp.dot(
            rotated, gate_matrix, precision=HIGHEST, preferred_element_type=jnp.float32
        )
    return gate_matrix


def apply_gate(two_site, gate_matrix):
    width = two_site.shape[1] // 2
    blocks = two_site.reshape(two_site.shape[0] // 2, 2, 2, width)
    mixed_gate = jnp.einsum(
        "pqtu,atuc->apqc", gate_matrix.reshape(2, 2, 2, 2), blocks, precision=HIGHEST
    )
    return mixed_gate.reshape(two_site.shape)


def matmul(left_side, right_side):
    return jnp.dot(left_side, right_side, precision=HIGHEST, preferred_element_type=jnp.float32)


def inner_rows(left_side, right_side):
    return lax.dot_general(
        left_side,
        right_side,
        (((0,), (0,)), ((), ())),
        precision=HIGHEST,
        preferred_element_type=jnp.float32,
    )


BLOCK = 128


def block_dot(left_side, right_side):
    return jnp.dot(left_side, right_side, precision=HIGHEST, preferred_element_type=jnp.float32)


def pick_pair(ref, base, offset, lanes):
    tile = ref[pl.ds(base, 8), lanes]
    sub = lax.broadcasted_iota(jnp.int32, tile.shape, 0)
    first = jnp.sum(jnp.where(sub == offset, tile, 0.0), axis=0, keepdims=True)
    second = jnp.sum(jnp.where(sub == offset + 1, tile, 0.0), axis=0, keepdims=True)
    return first, second


def lane_pick(row, lane, index):
    return jnp.sum(jnp.where(lane == index, row, 0.0), axis=1, keepdims=True)


def chol_inv_kernel(a_ref, w_ref, s_ref):
    n = a_ref.shape[0]
    nb = BLOCK
    blocks = n // nb
    s_ref[...] = a_ref[...]
    w_ref[...] = jnp.zeros((n, n), jnp.float32)
    eye_rows = lax.broadcasted_iota(jnp.int32, (nb, nb), 0)
    eye_cols = lax.broadcasted_iota(jnp.int32, (nb, nb), 1)
    eye = jnp.where(eye_rows == eye_cols, 1.0, 0.0).astype(jnp.float32)
    for p in range(blocks):
        r0 = p * nb
        diag = (slice(r0, r0 + nb), slice(r0, r0 + nb))
        w_ref[diag] = eye

        def step(t, carry):
            j = r0 + 2 * t
            base = pl.multiple_of(r0 + (t // 4) * 8, 8)
            offset = 2 * t - (t // 4) * 8
            lane = lax.broadcasted_iota(jnp.int32, (1, nb), 1) + r0
            row0, row1 = pick_pair(s_ref, base, offset, slice(r0, r0 + nb))
            a00 = lane_pick(row0, lane, j)
            a01 = lane_pick(row0, lane, j + 1)
            a11 = lane_pick(row1, lane, j + 1)
            inv0 = lax.rsqrt(a00)
            l10 = a01 * inv0
            inv1 = lax.rsqrt(a11 - l10 * l10)
            right0 = row0 * inv0
            right1 = (row1 - right0 * l10) * inv1
            later = lane > j + 1
            right0 = jnp.where(later, right0, 0.0)
            right1 = jnp.where(later, right1, 0.0)
            block = s_ref[diag]
            lane_d = lax.broadcasted_iota(jnp.int32, (nb, nb), 1) + r0
            col0 = jnp.sum(jnp.where(lane_d == j, block, 0.0), axis=1, keepdims=True)
            col1 = jnp.sum(jnp.where(lane_d == j + 1, block, 0.0), axis=1, keepdims=True)
            row_id = lax.broadcasted_iota(jnp.int32, (nb, 1), 0) + r0
            left0 = col0 * inv0
            left1 = (col1 - left0 * l10) * inv1
            below = row_id > j + 1
            down0 = jnp.where(below, left0, 0.0)
            down1 = jnp.where(below, left1, 0.0)
            updated = block - down0 * right0 - down1 * right1
            keep0 = jnp.where(row_id >= j, left0, 0.0)
            keep1 = jnp.where(row_id >= j + 1, left1, 0.0)
            s_ref[diag] = jnp.where(lane_d == j, keep0, jnp.where(lane_d == j + 1, keep1, updated))
            w0, w1 = pick_pair(w_ref, base, offset, slice(r0, r0 + nb))
            w0 = w0 * inv0
            w1 = (w1 - l10 * w0) * inv1
            w_block = w_ref[diag] - down0 * w0 - down1 * w1
            sub = lax.broadcasted_iota(jnp.int32, (nb, nb), 0) + r0
            w_ref[diag] = jnp.where(sub == j, w0, jnp.where(sub == j + 1, w1, w_block))
            return carry

        lax.fori_loop(0, nb // 2, step, 0)
        if p + 1 < blocks:
            panel = lax.dot_general(
                s_ref[r0 + nb:n, r0:r0 + nb], w_ref[diag], (((1,), (1,)), ((), ())),
                precision=HIGHEST, preferred_element_type=jnp.float32,
            )
            s_ref[r0 + nb:n, r0:r0 + nb] = panel
            s_ref[r0 + nb:n, r0 + nb:n] = s_ref[r0 + nb:n, r0 + nb:n] - lax.dot_general(
                panel, panel, (((1,), (1,)), ((), ())),
                precision=HIGHEST, preferred_element_type=jnp.float32,
            )
    for a in range(1, blocks):
        for b in range(a - 1, -1, -1):
            acc = jnp.zeros((nb, nb), jnp.float32)
            for k in range(b, a):
                acc = acc + block_dot(
                    s_ref[a * nb:(a + 1) * nb, k * nb:(k + 1) * nb],
                    w_ref[k * nb:(k + 1) * nb, b * nb:(b + 1) * nb],
                )
            w_ref[a * nb:(a + 1) * nb, b * nb:(b + 1) * nb] = -block_dot(
                w_ref[a * nb:(a + 1) * nb, a * nb:(a + 1) * nb], acc
            )


def chol_inv(gram):
    n = gram.shape[0]
    return pl.pallas_call(
        chol_inv_kernel,
        out_shape=jax.ShapeDtypeStruct((n, n), jnp.float32),
        in_specs=[pl.BlockSpec(memory_space=pltpu.VMEM)],
        out_specs=pl.BlockSpec(memory_space=pltpu.VMEM),
        scratch_shapes=[pltpu.VMEM((n, n), jnp.float32)],
    )(gram)

def orthonormal(sketched):
    gram_matrix = inner_rows(sketched, sketched)
    inverse_factor = chol_inv(gram_matrix)
    return lax.dot_general(
        sketched,
        inverse_factor,
        (((1,), (1,)), ((), ())),
        precision=HIGHEST,
        preferred_element_type=jnp.float32,
    )


def doubling_gather(block, axis):
    count = lax.axis_size(axis)
    index = lax.axis_index(axis)
    bits = count.bit_length() - 1
    gathered = block[None]
    for bit in reversed(range(bits)):
        mask = 1 << bit
        received = lax.ppermute(gathered, axis, [(source, source ^ mask) for source in range(count)])
        upper = (index & mask) != 0
        gathered = jnp.where(
            upper,
            jnp.stack([received, gathered]),
            jnp.stack([gathered, received]),
        )
    order = tuple(range(bits - 1, -1, -1)) + tuple(range(bits, gathered.ndim))
    gathered = jnp.transpose(gathered, order)
    return gathered.reshape((count * block.shape[0],) + block.shape[1:])


def on_device(left_core, right_core, gate_angles, sketch):
    width = left_core.shape[3]
    local_sites = left_core.shape[1]
    local_rows = 2 * local_sites
    both = jnp.stack([left_core[0], right_core[0]], axis=1)
    both = lax.all_gather(both, "row", axis=0, tiled=True)
    sites = both.shape[0]
    left_matrix = both[:, 0].reshape(2 * sites, width)
    right_matrix = both[:, 1].reshape(sites, 2 * width)
    two_site = matmul(left_matrix, right_matrix)
    two_site = apply_gate(two_site, build_gate(gate_angles[0]))
    full_sketch = doubling_gather(sketch, "bond")
    ortho_basis = orthonormal(matmul(two_site, full_sketch))
    for repeat in range(ITERS):
        projected = inner_rows(two_site, ortho_basis)
        ortho_basis = orthonormal(matmul(two_site, projected))
    start = lax.axis_index("row") * local_sites
    my_columns = lax.dynamic_slice_in_dim(ortho_basis, start, local_sites, axis=1)
    carried = inner_rows(my_columns, two_site)
    incoming = from_behind(carried, "bond", 1)
    incoming_matrix = incoming.reshape(local_rows, width)
    next_block = matmul(incoming_matrix, ortho_basis.reshape(sites, 2 * width))
    return next_block[None]


def solution(mesh):
    return jax.shard_map(
        on_device,
        mesh=mesh,
        in_specs=(
            P("bond", "row", None, None),
            P("bond", "row", None, None),
            P("bond", None),
            P("bond", None),
        ),
        out_specs=P("bond", "row", None),
        check_vma=False,
    )
```

```python
import jax
import jax.numpy as jnp
import numpy as np
from jax import lax
from jax.experimental import pallas as pl
from jax.experimental.pallas import tpu as pltpu
from jax.sharding import PartitionSpec as P

ITERS = 2


HIGHEST = lax.Precision.HIGHEST
PLANES = ((0, 1), (2, 3), (0, 2), (1, 3), (0, 3), (1, 2))


def from_behind(value, axis, steps):
    count = lax.axis_size(axis)
    initial, last = (max(0, -steps), min(count, count - steps))
    return lax.ppermute(value, axis, [(source, source + steps) for source in range(initial, last)])


def rotation(first_axis, second_axis, cosine, sine_value):
    unit = np.eye(4, dtype=np.float32)
    diag_part = np.outer(unit[first_axis], unit[first_axis]) + np.outer(
        unit[second_axis], unit[second_axis]
    )
    skew_part = np.outer(unit[second_axis], unit[first_axis]) - np.outer(
        unit[first_axis], unit[second_axis]
    )
    rest_part = np.eye(4, dtype=np.float32) - diag_part
    return (
        jnp.asarray(rest_part)
        + cosine * jnp.asarray(diag_part)
        + sine_value * jnp.asarray(skew_part)
    )


def build_gate(angles):
    gate_matrix = jnp.eye(4, dtype=jnp.float32)
    for number, plane in enumerate(PLANES):
        rotated = rotation(plane[0], plane[1], jnp.cos(angles[number]), jnp.sin(angles[number]))
        gate_matrix = jnp.dot(
            rotated, gate_matrix, precision=HIGHEST, preferred_element_type=jnp.float32
        )
    return gate_matrix


def apply_gate(two_site, gate_matrix):
    width = two_site.shape[1] // 2
    blocks = two_site.reshape(two_site.shape[0] // 2, 2, 2, width)
    mixed_gate = jnp.einsum(
        "pqtu,atuc->apqc", gate_matrix.reshape(2, 2, 2, 2), blocks, precision=HIGHEST
    )
    return mixed_gate.reshape(two_site.shape)


def matmul(left_side, right_side):
    return jnp.dot(left_side, right_side, precision=HIGHEST, preferred_element_type=jnp.float32)


def inner_rows(left_side, right_side):
    return lax.dot_general(
        left_side,
        right_side,
        (((0,), (0,)), ((), ())),
        precision=HIGHEST,
        preferred_element_type=jnp.float32,
    )


BLOCK = 128
PIVOTS = 4


def block_dot(left_side, right_side):
    return jnp.dot(left_side, right_side, precision=HIGHEST, preferred_element_type=jnp.float32)


def pick_rows(ref, base, offset, lanes, count):
    tile = ref[pl.ds(base, 8), lanes]
    sub = lax.broadcasted_iota(jnp.int32, tile.shape, 0)
    return [
        jnp.sum(jnp.where(sub == offset + i, tile, 0.0), axis=0, keepdims=True)
        for i in range(count)
    ]


def lane_pick(row, lane, index):
    return jnp.sum(jnp.where(lane == index, row, 0.0), axis=1, keepdims=True)


def chol_inv_kernel(a_ref, w_ref, s_ref):
    n = a_ref.shape[0]
    nb = BLOCK
    k = PIVOTS
    blocks = n // nb
    s_ref[...] = a_ref[...]
    w_ref[...] = jnp.zeros((n, n), jnp.float32)
    eye_rows = lax.broadcasted_iota(jnp.int32, (nb, nb), 0)
    eye_cols = lax.broadcasted_iota(jnp.int32, (nb, nb), 1)
    eye = jnp.where(eye_rows == eye_cols, 1.0, 0.0).astype(jnp.float32)
    per_tile = 8 // k
    for p in range(blocks):
        r0 = p * nb
        diag = (slice(r0, r0 + nb), slice(r0, r0 + nb))
        w_ref[diag] = eye

        def step(t, carry):
            j = r0 + k * t
            base = pl.multiple_of(r0 + (t // per_tile) * 8, 8)
            offset = k * t - (t // per_tile) * 8
            lane = lax.broadcasted_iota(jnp.int32, (1, nb), 1) + r0
            rows = pick_rows(s_ref, base, offset, slice(r0, r0 + nb), k)
            w_rows = pick_rows(w_ref, base, offset, slice(r0, r0 + nb), k)
            block = s_ref[diag]
            lane_d = lax.broadcasted_iota(jnp.int32, (nb, nb), 1) + r0
            cols = [
                jnp.sum(jnp.where(lane_d == j + i, block, 0.0), axis=1, keepdims=True)
                for i in range(k)
            ]
            rights, lefts = [], []
            for i in range(k):
                inv = lax.rsqrt(lane_pick(rows[i], lane, j + i))
                right = rows[i] * inv
                left = cols[i] * inv
                w_rows[i] = w_rows[i] * inv
                for later in range(i + 1, k):
                    factor = lane_pick(right, lane, j + later)
                    rows[later] = rows[later] - factor * right
                    cols[later] = cols[later] - factor * left
                    w_rows[later] = w_rows[later] - factor * w_rows[i]
                rights.append(right)
                lefts.append(left)
            row_id = lax.broadcasted_iota(jnp.int32, (nb, 1), 0) + r0
            after = lane > j + k - 1
            below = row_id > j + k - 1
            updated = block
            w_block = w_ref[diag]
            for i in range(k):
                down = jnp.where(below, lefts[i], 0.0)
                updated = updated - down * jnp.where(after, rights[i], 0.0)
                w_block = w_block - down * w_rows[i]
            sub = lax.broadcasted_iota(jnp.int32, (nb, nb), 0) + r0
            for i in range(k):
                keep = jnp.where(row_id >= j + i, lefts[i], 0.0)
                updated = jnp.where(lane_d == j + i, keep, updated)
                w_block = jnp.where(sub == j + i, w_rows[i], w_block)
            s_ref[diag] = updated
            w_ref[diag] = w_block
            return carry

        lax.fori_loop(0, nb // k, step, 0)
        if p + 1 < blocks:
            panel = lax.dot_general(
                s_ref[r0 + nb:n, r0:r0 + nb], w_ref[diag], (((1,), (1,)), ((), ())),
                precision=HIGHEST, preferred_element_type=jnp.float32,
            )
            s_ref[r0 + nb:n, r0:r0 + nb] = panel
            s_ref[r0 + nb:n, r0 + nb:n] = s_ref[r0 + nb:n, r0 + nb:n] - lax.dot_general(
                panel, panel, (((1,), (1,)), ((), ())),
                precision=HIGHEST, preferred_element_type=jnp.float32,
            )
    for a in range(1, blocks):
        for b in range(a - 1, -1, -1):
            acc = jnp.zeros((nb, nb), jnp.float32)
            for m in range(b, a):
                acc = acc + block_dot(
                    s_ref[a * nb:(a + 1) * nb, m * nb:(m + 1) * nb],
                    w_ref[m * nb:(m + 1) * nb, b * nb:(b + 1) * nb],
                )
            w_ref[a * nb:(a + 1) * nb, b * nb:(b + 1) * nb] = -block_dot(
                w_ref[a * nb:(a + 1) * nb, a * nb:(a + 1) * nb], acc
            )


def chol_inv(gram):
    n = gram.shape[0]
    return pl.pallas_call(
        chol_inv_kernel,
        out_shape=jax.ShapeDtypeStruct((n, n), jnp.float32),
        in_specs=[pl.BlockSpec(memory_space=pltpu.VMEM)],
        out_specs=pl.BlockSpec(memory_space=pltpu.VMEM),
        scratch_shapes=[pltpu.VMEM((n, n), jnp.float32)],
    )(gram)

def orthonormal(sketched):
    gram_matrix = inner_rows(sketched, sketched)
    inverse_factor = chol_inv(gram_matrix)
    return lax.dot_general(
        sketched,
        inverse_factor,
        (((1,), (1,)), ((), ())),
        precision=HIGHEST,
        preferred_element_type=jnp.float32,
    )


def doubling_gather(block, axis):
    count = lax.axis_size(axis)
    index = lax.axis_index(axis)
    bits = count.bit_length() - 1
    gathered = block[None]
    for bit in reversed(range(bits)):
        mask = 1 << bit
        received = lax.ppermute(gathered, axis, [(source, source ^ mask) for source in range(count)])
        upper = (index & mask) != 0
        gathered = jnp.where(
            upper,
            jnp.stack([received, gathered]),
            jnp.stack([gathered, received]),
        )
    order = tuple(range(bits - 1, -1, -1)) + tuple(range(bits, gathered.ndim))
    gathered = jnp.transpose(gathered, order)
    return gathered.reshape((count * block.shape[0],) + block.shape[1:])


def on_device(left_core, right_core, gate_angles, sketch):
    width = left_core.shape[3]
    local_sites = left_core.shape[1]
    local_rows = 2 * local_sites
    both = jnp.stack([left_core[0], right_core[0]], axis=1)
    both = lax.all_gather(both, "row", axis=0, tiled=True)
    sites = both.shape[0]
    left_matrix = both[:, 0].reshape(2 * sites, width)
    right_matrix = both[:, 1].reshape(sites, 2 * width)
    two_site = matmul(left_matrix, right_matrix)
    two_site = apply_gate(two_site, build_gate(gate_angles[0]))
    full_sketch = doubling_gather(sketch, "bond")
    ortho_basis = orthonormal(matmul(two_site, full_sketch))
    for repeat in range(ITERS):
        projected = inner_rows(two_site, ortho_basis)
        ortho_basis = orthonormal(matmul(two_site, projected))
    start = lax.axis_index("row") * local_sites
    my_columns = lax.dynamic_slice_in_dim(ortho_basis, start, local_sites, axis=1)
    carried = inner_rows(my_columns, two_site)
    incoming = from_behind(carried, "bond", 1)
    incoming_matrix = incoming.reshape(local_rows, width)
    next_block = matmul(incoming_matrix, ortho_basis.reshape(sites, 2 * width))
    return next_block[None]


def solution(mesh):
    return jax.shard_map(
        on_device,
        mesh=mesh,
        in_specs=(
            P("bond", "row", None, None),
            P("bond", "row", None, None),
            P("bond", None),
            P("bond", None),
        ),
        out_specs=P("bond", "row", None),
        check_vma=False,
    )
```

```python
import jax
import jax.numpy as jnp
import numpy as np
from jax import lax
from jax.experimental import pallas as pl
from jax.experimental.pallas import tpu as pltpu
from jax.sharding import PartitionSpec as P

ITERS = 2


HIGHEST = lax.Precision.HIGHEST
PLANES = ((0, 1), (2, 3), (0, 2), (1, 3), (0, 3), (1, 2))


def from_behind(value, axis, steps):
    count = lax.axis_size(axis)
    initial, last = (max(0, -steps), min(count, count - steps))
    return lax.ppermute(value, axis, [(source, source + steps) for source in range(initial, last)])


def rotation(first_axis, second_axis, cosine, sine_value):
    unit = np.eye(4, dtype=np.float32)
    diag_part = np.outer(unit[first_axis], unit[first_axis]) + np.outer(
        unit[second_axis], unit[second_axis]
    )
    skew_part = np.outer(unit[second_axis], unit[first_axis]) - np.outer(
        unit[first_axis], unit[second_axis]
    )
    rest_part = np.eye(4, dtype=np.float32) - diag_part
    return (
        jnp.asarray(rest_part)
        + cosine * jnp.asarray(diag_part)
        + sine_value * jnp.asarray(skew_part)
    )


def build_gate(angles):
    gate_matrix = jnp.eye(4, dtype=jnp.float32)
    for number, plane in enumerate(PLANES):
        rotated = rotation(plane[0], plane[1], jnp.cos(angles[number]), jnp.sin(angles[number]))
        gate_matrix = jnp.dot(
            rotated, gate_matrix, precision=HIGHEST, preferred_element_type=jnp.float32
        )
    return gate_matrix


def apply_gate(two_site, gate_matrix):
    width = two_site.shape[1] // 2
    blocks = two_site.reshape(two_site.shape[0] // 2, 2, 2, width)
    mixed_gate = jnp.einsum(
        "pqtu,atuc->apqc", gate_matrix.reshape(2, 2, 2, 2), blocks, precision=HIGHEST
    )
    return mixed_gate.reshape(two_site.shape)


def matmul(left_side, right_side):
    return jnp.dot(left_side, right_side, precision=HIGHEST, preferred_element_type=jnp.float32)


def inner_rows(left_side, right_side):
    return lax.dot_general(
        left_side,
        right_side,
        (((0,), (0,)), ((), ())),
        precision=HIGHEST,
        preferred_element_type=jnp.float32,
    )


BLOCK = 128


def block_dot(left_side, right_side):
    return jnp.dot(left_side, right_side, precision=HIGHEST, preferred_element_type=jnp.float32)


def pick_pair(ref, base, offset, lanes):
    tile = ref[pl.ds(base, 8), lanes]
    sub = lax.broadcasted_iota(jnp.int32, tile.shape, 0)
    first = jnp.sum(jnp.where(sub == offset, tile, 0.0), axis=0, keepdims=True)
    second = jnp.sum(jnp.where(sub == offset + 1, tile, 0.0), axis=0, keepdims=True)
    return first, second


def lane_pick(row, lane, index):
    return jnp.sum(jnp.where(lane == index, row, 0.0), axis=1, keepdims=True)


def chol_inv_kernel(a_ref, w_ref, s_ref):
    n = a_ref.shape[0]
    nb = BLOCK
    blocks = n // nb
    s_ref[...] = a_ref[...]
    w_ref[...] = jnp.zeros((n, n), jnp.float32)
    eye_rows = lax.broadcasted_iota(jnp.int32, (nb, nb), 0)
    eye_cols = lax.broadcasted_iota(jnp.int32, (nb, nb), 1)
    eye = jnp.where(eye_rows == eye_cols, 1.0, 0.0).astype(jnp.float32)
    for p in range(blocks):
        r0 = p * nb
        diag = (slice(r0, r0 + nb), slice(r0, r0 + nb))
        w_ref[diag] = eye

        def step(t, carry):
            j = r0 + 2 * t
            base = pl.multiple_of(r0 + (t // 4) * 8, 8)
            offset = 2 * t - (t // 4) * 8
            lane = lax.broadcasted_iota(jnp.int32, (1, nb), 1) + r0
            row0, row1 = pick_pair(s_ref, base, offset, slice(r0, r0 + nb))
            a00 = lane_pick(row0, lane, j)
            a01 = lane_pick(row0, lane, j + 1)
            a11 = lane_pick(row1, lane, j + 1)
            inv0 = lax.rsqrt(a00)
            l10 = a01 * inv0
            inv1 = lax.rsqrt(a11 - l10 * l10)
            right0 = row0 * inv0
            right1 = (row1 - right0 * l10) * inv1
            later = lane > j + 1
            right0 = jnp.where(later, right0, 0.0)
            right1 = jnp.where(later, right1, 0.0)
            block = s_ref[diag]
            lane_d = lax.broadcasted_iota(jnp.int32, (nb, nb), 1) + r0
            col0 = jnp.sum(jnp.where(lane_d == j, block, 0.0), axis=1, keepdims=True)
            col1 = jnp.sum(jnp.where(lane_d == j + 1, block, 0.0), axis=1, keepdims=True)
            row_id = lax.broadcasted_iota(jnp.int32, (nb, 1), 0) + r0
            left0 = col0 * inv0
            left1 = (col1 - left0 * l10) * inv1
            below = row_id > j + 1
            down0 = jnp.where(below, left0, 0.0)
            down1 = jnp.where(below, left1, 0.0)
            updated = block - down0 * right0 - down1 * right1
            keep0 = jnp.where(row_id >= j, left0, 0.0)
            keep1 = jnp.where(row_id >= j + 1, left1, 0.0)
            s_ref[diag] = jnp.where(lane_d == j, keep0, jnp.where(lane_d == j + 1, keep1, updated))
            w0, w1 = pick_pair(w_ref, base, offset, slice(r0, r0 + nb))
            w0 = w0 * inv0
            w1 = (w1 - l10 * w0) * inv1
            w_block = w_ref[diag] - down0 * w0 - down1 * w1
            sub = lax.broadcasted_iota(jnp.int32, (nb, nb), 0) + r0
            w_ref[diag] = jnp.where(sub == j, w0, jnp.where(sub == j + 1, w1, w_block))
            return carry

        lax.fori_loop(0, nb // 2, step, 0)
        if p + 1 < blocks:
            panel = lax.dot_general(
                s_ref[r0 + nb:n, r0:r0 + nb], w_ref[diag], (((1,), (1,)), ((), ())),
                precision=HIGHEST, preferred_element_type=jnp.float32,
            )
            s_ref[r0 + nb:n, r0:r0 + nb] = panel
            s_ref[r0 + nb:n, r0 + nb:n] = s_ref[r0 + nb:n, r0 + nb:n] - lax.dot_general(
                panel, panel, (((1,), (1,)), ((), ())),
                precision=HIGHEST, preferred_element_type=jnp.float32,
            )
    for a in range(1, blocks):
        for b in range(a - 1, -1, -1):
            acc = jnp.zeros((nb, nb), jnp.float32)
            for k in range(b, a):
                acc = acc + block_dot(
                    s_ref[a * nb:(a + 1) * nb, k * nb:(k + 1) * nb],
                    w_ref[k * nb:(k + 1) * nb, b * nb:(b + 1) * nb],
                )
            w_ref[a * nb:(a + 1) * nb, b * nb:(b + 1) * nb] = -block_dot(
                w_ref[a * nb:(a + 1) * nb, a * nb:(a + 1) * nb], acc
            )


def chol_inv(gram):
    n = gram.shape[0]
    return pl.pallas_call(
        chol_inv_kernel,
        out_shape=jax.ShapeDtypeStruct((n, n), jnp.float32),
        in_specs=[pl.BlockSpec(memory_space=pltpu.VMEM)],
        out_specs=pl.BlockSpec(memory_space=pltpu.VMEM),
        scratch_shapes=[pltpu.VMEM((n, n), jnp.float32)],
    )(gram)

def orthonormal(sketched):
    gram_matrix = inner_rows(sketched, sketched)
    inverse_factor = chol_inv(gram_matrix)
    return lax.dot_general(
        sketched,
        inverse_factor,
        (((1,), (1,)), ((), ())),
        precision=HIGHEST,
        preferred_element_type=jnp.float32,
    )


def doubling_gather(block, axis):
    count = lax.axis_size(axis)
    index = lax.axis_index(axis)
    bits = count.bit_length() - 1
    gathered = block[None]
    for bit in reversed(range(bits)):
        mask = 1 << bit
        received = lax.ppermute(gathered, axis, [(source, source ^ mask) for source in range(count)])
        upper = (index & mask) != 0
        gathered = jnp.where(
            upper,
            jnp.stack([received, gathered]),
            jnp.stack([gathered, received]),
        )
    order = tuple(range(bits - 1, -1, -1)) + tuple(range(bits, gathered.ndim))
    gathered = jnp.transpose(gathered, order)
    return gathered.reshape((count * block.shape[0],) + block.shape[1:])


def on_device(left_core, right_core, gate_angles, sketch):
    width = left_core.shape[3]
    local_sites = left_core.shape[1]
    local_rows = 2 * local_sites
    left_full = lax.all_gather(left_core[0], "row", axis=0, tiled=True)
    right_full = doubling_gather(right_core[0], "row")
    sites = left_full.shape[0]
    left_matrix = left_full.reshape(2 * sites, width)
    right_matrix = right_full.reshape(sites, 2 * width)
    two_site = matmul(left_matrix, right_matrix)
    two_site = apply_gate(two_site, build_gate(gate_angles[0]))
    full_sketch = doubling_gather(sketch, "bond")
    ortho_basis = orthonormal(matmul(two_site, full_sketch))
    for repeat in range(ITERS):
        projected = inner_rows(two_site, ortho_basis)
        ortho_basis = orthonormal(matmul(two_site, projected))
    start = lax.axis_index("row") * local_sites
    my_columns = lax.dynamic_slice_in_dim(ortho_basis, start, local_sites, axis=1)
    carried = inner_rows(my_columns, two_site)
    incoming = from_behind(carried, "bond", 1)
    incoming_matrix = incoming.reshape(local_rows, width)
    next_block = matmul(incoming_matrix, ortho_basis.reshape(sites, 2 * width))
    return next_block[None]


def solution(mesh):
    return jax.shard_map(
        on_device,
        mesh=mesh,
        in_specs=(
            P("bond", "row", None, None),
            P("bond", "row", None, None),
            P("bond", None),
            P("bond", None),
        ),
        out_specs=P("bond", "row", None),
        check_vma=False,
    )
```

```python
import jax
import jax.numpy as jnp
import numpy as np
from jax import lax
from jax.experimental import pallas as pl
from jax.experimental.pallas import tpu as pltpu
from jax.sharding import PartitionSpec as P

ITERS = 2


HIGHEST = lax.Precision.HIGHEST
PLANES = ((0, 1), (2, 3), (0, 2), (1, 3), (0, 3), (1, 2))


def from_behind(value, axis, steps):
    count = lax.axis_size(axis)
    initial, last = (max(0, -steps), min(count, count - steps))
    return lax.ppermute(value, axis, [(source, source + steps) for source in range(initial, last)])


def rotation(first_axis, second_axis, cosine, sine_value):
    unit = np.eye(4, dtype=np.float32)
    diag_part = np.outer(unit[first_axis], unit[first_axis]) + np.outer(
        unit[second_axis], unit[second_axis]
    )
    skew_part = np.outer(unit[second_axis], unit[first_axis]) - np.outer(
        unit[first_axis], unit[second_axis]
    )
    rest_part = np.eye(4, dtype=np.float32) - diag_part
    return (
        jnp.asarray(rest_part)
        + cosine * jnp.asarray(diag_part)
        + sine_value * jnp.asarray(skew_part)
    )


def build_gate(angles):
    gate_matrix = jnp.eye(4, dtype=jnp.float32)
    for number, plane in enumerate(PLANES):
        rotated = rotation(plane[0], plane[1], jnp.cos(angles[number]), jnp.sin(angles[number]))
        gate_matrix = jnp.dot(
            rotated, gate_matrix, precision=HIGHEST, preferred_element_type=jnp.float32
        )
    return gate_matrix


def apply_gate(two_site, gate_matrix):
    width = two_site.shape[1] // 2
    blocks = two_site.reshape(two_site.shape[0] // 2, 2, 2, width)
    mixed_gate = jnp.einsum(
        "pqtu,atuc->apqc", gate_matrix.reshape(2, 2, 2, 2), blocks, precision=HIGHEST
    )
    return mixed_gate.reshape(two_site.shape)


def matmul(left_side, right_side):
    return jnp.dot(left_side, right_side, precision=HIGHEST, preferred_element_type=jnp.float32)


def inner_rows(left_side, right_side):
    return lax.dot_general(
        left_side,
        right_side,
        (((0,), (0,)), ((), ())),
        precision=HIGHEST,
        preferred_element_type=jnp.float32,
    )


BLOCK = 128


def block_dot(left_side, right_side):
    return jnp.dot(left_side, right_side, precision=HIGHEST, preferred_element_type=jnp.float32)


def pick_pair(ref, base, offset, lanes):
    tile = ref[pl.ds(base, 8), lanes]
    sub = lax.broadcasted_iota(jnp.int32, tile.shape, 0)
    first = jnp.sum(jnp.where(sub == offset, tile, 0.0), axis=0, keepdims=True)
    second = jnp.sum(jnp.where(sub == offset + 1, tile, 0.0), axis=0, keepdims=True)
    return first, second


def lane_pick(row, lane, index):
    return jnp.sum(jnp.where(lane == index, row, 0.0), axis=1, keepdims=True)


def chol_inv_kernel(a_ref, w_ref, s_ref):
    n = a_ref.shape[0]
    nb = BLOCK
    blocks = n // nb
    s_ref[...] = a_ref[...]
    w_ref[...] = jnp.zeros((n, n), jnp.float32)
    eye_rows = lax.broadcasted_iota(jnp.int32, (nb, nb), 0)
    eye_cols = lax.broadcasted_iota(jnp.int32, (nb, nb), 1)
    eye = jnp.where(eye_rows == eye_cols, 1.0, 0.0).astype(jnp.float32)
    for p in range(blocks):
        r0 = p * nb
        diag = (slice(r0, r0 + nb), slice(r0, r0 + nb))
        w_ref[diag] = eye

        def step(t, carry):
            j = r0 + 2 * t
            base = pl.multiple_of(r0 + (t // 4) * 8, 8)
            offset = 2 * t - (t // 4) * 8
            lane = lax.broadcasted_iota(jnp.int32, (1, nb), 1) + r0
            row0, row1 = pick_pair(s_ref, base, offset, slice(r0, r0 + nb))
            a00 = lane_pick(row0, lane, j)
            a01 = lane_pick(row0, lane, j + 1)
            a11 = lane_pick(row1, lane, j + 1)
            inv0 = lax.rsqrt(a00)
            l10 = a01 * inv0
            inv1 = lax.rsqrt(a11 - l10 * l10)
            right0 = row0 * inv0
            right1 = (row1 - right0 * l10) * inv1
            later = lane > j + 1
            right0 = jnp.where(later, right0, 0.0)
            right1 = jnp.where(later, right1, 0.0)
            block = s_ref[diag]
            lane_d = lax.broadcasted_iota(jnp.int32, (nb, nb), 1) + r0
            col0 = jnp.sum(jnp.where(lane_d == j, block, 0.0), axis=1, keepdims=True)
            col1 = jnp.sum(jnp.where(lane_d == j + 1, block, 0.0), axis=1, keepdims=True)
            row_id = lax.broadcasted_iota(jnp.int32, (nb, 1), 0) + r0
            left0 = col0 * inv0
            left1 = (col1 - left0 * l10) * inv1
            below = row_id > j + 1
            down0 = jnp.where(below, left0, 0.0)
            down1 = jnp.where(below, left1, 0.0)
            updated = block - down0 * right0 - down1 * right1
            keep0 = jnp.where(row_id >= j, left0, 0.0)
            keep1 = jnp.where(row_id >= j + 1, left1, 0.0)
            s_ref[diag] = jnp.where(lane_d == j, keep0, jnp.where(lane_d == j + 1, keep1, updated))
            w0, w1 = pick_pair(w_ref, base, offset, slice(r0, r0 + nb))
            w0 = w0 * inv0
            w1 = (w1 - l10 * w0) * inv1
            w_block = w_ref[diag] - down0 * w0 - down1 * w1
            sub = lax.broadcasted_iota(jnp.int32, (nb, nb), 0) + r0
            w_ref[diag] = jnp.where(sub == j, w0, jnp.where(sub == j + 1, w1, w_block))
            return carry

        lax.fori_loop(0, nb // 2, step, 0, unroll=2)
        if p + 1 < blocks:
            panel = lax.dot_general(
                s_ref[r0 + nb:n, r0:r0 + nb], w_ref[diag], (((1,), (1,)), ((), ())),
                precision=HIGHEST, preferred_element_type=jnp.float32,
            )
            s_ref[r0 + nb:n, r0:r0 + nb] = panel
            s_ref[r0 + nb:n, r0 + nb:n] = s_ref[r0 + nb:n, r0 + nb:n] - lax.dot_general(
                panel, panel, (((1,), (1,)), ((), ())),
                precision=HIGHEST, preferred_element_type=jnp.float32,
            )
    for a in range(1, blocks):
        for b in range(a - 1, -1, -1):
            acc = jnp.zeros((nb, nb), jnp.float32)
            for k in range(b, a):
                acc = acc + block_dot(
                    s_ref[a * nb:(a + 1) * nb, k * nb:(k + 1) * nb],
                    w_ref[k * nb:(k + 1) * nb, b * nb:(b + 1) * nb],
                )
            w_ref[a * nb:(a + 1) * nb, b * nb:(b + 1) * nb] = -block_dot(
                w_ref[a * nb:(a + 1) * nb, a * nb:(a + 1) * nb], acc
            )


def chol_inv(gram):
    n = gram.shape[0]
    return pl.pallas_call(
        chol_inv_kernel,
        out_shape=jax.ShapeDtypeStruct((n, n), jnp.float32),
        in_specs=[pl.BlockSpec(memory_space=pltpu.VMEM)],
        out_specs=pl.BlockSpec(memory_space=pltpu.VMEM),
        scratch_shapes=[pltpu.VMEM((n, n), jnp.float32)],
    )(gram)

def orthonormal(sketched):
    gram_matrix = inner_rows(sketched, sketched)
    inverse_factor = chol_inv(gram_matrix)
    return lax.dot_general(
        sketched,
        inverse_factor,
        (((1,), (1,)), ((), ())),
        precision=HIGHEST,
        preferred_element_type=jnp.float32,
    )


def doubling_gather(block, axis):
    count = lax.axis_size(axis)
    index = lax.axis_index(axis)
    bits = count.bit_length() - 1
    gathered = block[None]
    for bit in reversed(range(bits)):
        mask = 1 << bit
        received = lax.ppermute(gathered, axis, [(source, source ^ mask) for source in range(count)])
        upper = (index & mask) != 0
        gathered = jnp.where(
            upper,
            jnp.stack([received, gathered]),
            jnp.stack([gathered, received]),
        )
    order = tuple(range(bits - 1, -1, -1)) + tuple(range(bits, gathered.ndim))
    gathered = jnp.transpose(gathered, order)
    return gathered.reshape((count * block.shape[0],) + block.shape[1:])


def on_device(left_core, right_core, gate_angles, sketch):
    width = left_core.shape[3]
    local_sites = left_core.shape[1]
    local_rows = 2 * local_sites
    both = jnp.stack([left_core[0], right_core[0]], axis=1)
    both = lax.all_gather(both, "row", axis=0, tiled=True)
    sites = both.shape[0]
    left_matrix = both[:, 0].reshape(2 * sites, width)
    right_matrix = both[:, 1].reshape(sites, 2 * width)
    two_site = matmul(left_matrix, right_matrix)
    two_site = apply_gate(two_site, build_gate(gate_angles[0]))
    full_sketch = doubling_gather(sketch, "bond")
    ortho_basis = orthonormal(matmul(two_site, full_sketch))
    for repeat in range(ITERS):
        projected = inner_rows(two_site, ortho_basis)
        ortho_basis = orthonormal(matmul(two_site, projected))
    start = lax.axis_index("row") * local_sites
    my_columns = lax.dynamic_slice_in_dim(ortho_basis, start, local_sites, axis=1)
    carried = inner_rows(my_columns, two_site)
    incoming = from_behind(carried, "bond", 1)
    incoming_matrix = incoming.reshape(local_rows, width)
    next_block = matmul(incoming_matrix, ortho_basis.reshape(sites, 2 * width))
    return next_block[None]


def solution(mesh):
    return jax.shard_map(
        on_device,
        mesh=mesh,
        in_specs=(
            P("bond", "row", None, None),
            P("bond", "row", None, None),
            P("bond", None),
            P("bond", None),
        ),
        out_specs=P("bond", "row", None),
        check_vma=False,
    )
```

```python
import jax
import jax.numpy as jnp
import numpy as np
from jax import lax
from jax.experimental import pallas as pl
from jax.experimental.pallas import tpu as pltpu
from jax.sharding import PartitionSpec as P

ITERS = 2


HIGHEST = lax.Precision.HIGHEST
PLANES = ((0, 1), (2, 3), (0, 2), (1, 3), (0, 3), (1, 2))


def from_behind(value, axis, steps):
    count = lax.axis_size(axis)
    initial, last = (max(0, -steps), min(count, count - steps))
    return lax.ppermute(value, axis, [(source, source + steps) for source in range(initial, last)])


def rotation(first_axis, second_axis, cosine, sine_value):
    unit = np.eye(4, dtype=np.float32)
    diag_part = np.outer(unit[first_axis], unit[first_axis]) + np.outer(
        unit[second_axis], unit[second_axis]
    )
    skew_part = np.outer(unit[second_axis], unit[first_axis]) - np.outer(
        unit[first_axis], unit[second_axis]
    )
    rest_part = np.eye(4, dtype=np.float32) - diag_part
    return (
        jnp.asarray(rest_part)
        + cosine * jnp.asarray(diag_part)
        + sine_value * jnp.asarray(skew_part)
    )


def build_gate(angles):
    gate_matrix = jnp.eye(4, dtype=jnp.float32)
    for number, plane in enumerate(PLANES):
        rotated = rotation(plane[0], plane[1], jnp.cos(angles[number]), jnp.sin(angles[number]))
        gate_matrix = jnp.dot(
            rotated, gate_matrix, precision=HIGHEST, preferred_element_type=jnp.float32
        )
    return gate_matrix


def apply_gate(two_site, gate_matrix):
    width = two_site.shape[1] // 2
    blocks = two_site.reshape(two_site.shape[0] // 2, 2, 2, width)
    gate_parts = gate_matrix.reshape(2, 2, 2, 2)
    mixed_gate = sum(
        gate_parts[None, :, :, t, u, None] * blocks[:, None, None, t, u, :]
        for t in range(2)
        for u in range(2)
    )
    return mixed_gate.reshape(two_site.shape)


def matmul(left_side, right_side):
    return jnp.dot(left_side, right_side, precision=HIGHEST, preferred_element_type=jnp.float32)


def inner_rows(left_side, right_side):
    return lax.dot_general(
        left_side,
        right_side,
        (((0,), (0,)), ((), ())),
        precision=HIGHEST,
        preferred_element_type=jnp.float32,
    )


BLOCK = 128


def block_dot(left_side, right_side):
    return jnp.dot(left_side, right_side, precision=HIGHEST, preferred_element_type=jnp.float32)


def pick_pair(ref, base, offset, lanes):
    tile = ref[pl.ds(base, 8), lanes]
    sub = lax.broadcasted_iota(jnp.int32, tile.shape, 0)
    first = jnp.sum(jnp.where(sub == offset, tile, 0.0), axis=0, keepdims=True)
    second = jnp.sum(jnp.where(sub == offset + 1, tile, 0.0), axis=0, keepdims=True)
    return first, second


def lane_pick(row, lane, index):
    return jnp.sum(jnp.where(lane == index, row, 0.0), axis=1, keepdims=True)


def chol_inv_kernel(a_ref, w_ref, s_ref):
    n = a_ref.shape[0]
    nb = BLOCK
    blocks = n // nb
    s_ref[...] = a_ref[...]
    w_ref[...] = jnp.zeros((n, n), jnp.float32)
    eye_rows = lax.broadcasted_iota(jnp.int32, (nb, nb), 0)
    eye_cols = lax.broadcasted_iota(jnp.int32, (nb, nb), 1)
    eye = jnp.where(eye_rows == eye_cols, 1.0, 0.0).astype(jnp.float32)
    for p in range(blocks):
        r0 = p * nb
        diag = (slice(r0, r0 + nb), slice(r0, r0 + nb))
        w_ref[diag] = eye

        def step(t, carry):
            j = r0 + 2 * t
            base = pl.multiple_of(r0 + (t // 4) * 8, 8)
            offset = 2 * t - (t // 4) * 8
            lane = lax.broadcasted_iota(jnp.int32, (1, nb), 1) + r0
            row0, row1 = pick_pair(s_ref, base, offset, slice(r0, r0 + nb))
            a00 = lane_pick(row0, lane, j)
            a01 = lane_pick(row0, lane, j + 1)
            a11 = lane_pick(row1, lane, j + 1)
            inv0 = lax.rsqrt(a00)
            l10 = a01 * inv0
            inv1 = lax.rsqrt(a11 - l10 * l10)
            right0 = row0 * inv0
            right1 = (row1 - right0 * l10) * inv1
            later = lane > j + 1
            right0 = jnp.where(later, right0, 0.0)
            right1 = jnp.where(later, right1, 0.0)
            block = s_ref[diag]
            lane_d = lax.broadcasted_iota(jnp.int32, (nb, nb), 1) + r0
            col0 = jnp.sum(jnp.where(lane_d == j, block, 0.0), axis=1, keepdims=True)
            col1 = jnp.sum(jnp.where(lane_d == j + 1, block, 0.0), axis=1, keepdims=True)
            row_id = lax.broadcasted_iota(jnp.int32, (nb, 1), 0) + r0
            left0 = col0 * inv0
            left1 = (col1 - left0 * l10) * inv1
            below = row_id > j + 1
            down0 = jnp.where(below, left0, 0.0)
            down1 = jnp.where(below, left1, 0.0)
            updated = block - down0 * right0 - down1 * right1
            keep0 = jnp.where(row_id >= j, left0, 0.0)
            keep1 = jnp.where(row_id >= j + 1, left1, 0.0)
            s_ref[diag] = jnp.where(lane_d == j, keep0, jnp.where(lane_d == j + 1, keep1, updated))
            w0, w1 = pick_pair(w_ref, base, offset, slice(r0, r0 + nb))
            w0 = w0 * inv0
            w1 = (w1 - l10 * w0) * inv1
            w_block = w_ref[diag] - down0 * w0 - down1 * w1
            sub = lax.broadcasted_iota(jnp.int32, (nb, nb), 0) + r0
            w_ref[diag] = jnp.where(sub == j, w0, jnp.where(sub == j + 1, w1, w_block))
            return carry

        lax.fori_loop(0, nb // 2, step, 0, unroll=2)
        if p + 1 < blocks:
            panel = lax.dot_general(
                s_ref[r0 + nb:n, r0:r0 + nb], w_ref[diag], (((1,), (1,)), ((), ())),
                precision=HIGHEST, preferred_element_type=jnp.float32,
            )
            s_ref[r0 + nb:n, r0:r0 + nb] = panel
            s_ref[r0 + nb:n, r0 + nb:n] = s_ref[r0 + nb:n, r0 + nb:n] - lax.dot_general(
                panel, panel, (((1,), (1,)), ((), ())),
                precision=HIGHEST, preferred_element_type=jnp.float32,
            )
    for a in range(1, blocks):
        for b in range(a - 1, -1, -1):
            acc = jnp.zeros((nb, nb), jnp.float32)
            for k in range(b, a):
                acc = acc + block_dot(
                    s_ref[a * nb:(a + 1) * nb, k * nb:(k + 1) * nb],
                    w_ref[k * nb:(k + 1) * nb, b * nb:(b + 1) * nb],
                )
            w_ref[a * nb:(a + 1) * nb, b * nb:(b + 1) * nb] = -block_dot(
                w_ref[a * nb:(a + 1) * nb, a * nb:(a + 1) * nb], acc
            )


def chol_inv(gram):
    n = gram.shape[0]
    return pl.pallas_call(
        chol_inv_kernel,
        out_shape=jax.ShapeDtypeStruct((n, n), jnp.float32),
        in_specs=[pl.BlockSpec(memory_space=pltpu.VMEM)],
        out_specs=pl.BlockSpec(memory_space=pltpu.VMEM),
        scratch_shapes=[pltpu.VMEM((n, n), jnp.float32)],
    )(gram)

def orthonormal(sketched):
    gram_matrix = inner_rows(sketched, sketched)
    inverse_factor = chol_inv(gram_matrix)
    return lax.dot_general(
        sketched,
        inverse_factor,
        (((1,), (1,)), ((), ())),
        precision=HIGHEST,
        preferred_element_type=jnp.float32,
    )


def doubling_gather(block, axis):
    count = lax.axis_size(axis)
    index = lax.axis_index(axis)
    bits = count.bit_length() - 1
    gathered = block[None]
    for bit in reversed(range(bits)):
        mask = 1 << bit
        received = lax.ppermute(gathered, axis, [(source, source ^ mask) for source in range(count)])
        upper = (index & mask) != 0
        gathered = jnp.where(
            upper,
            jnp.stack([received, gathered]),
            jnp.stack([gathered, received]),
        )
    order = tuple(range(bits - 1, -1, -1)) + tuple(range(bits, gathered.ndim))
    gathered = jnp.transpose(gathered, order)
    return gathered.reshape((count * block.shape[0],) + block.shape[1:])


def on_device(left_core, right_core, gate_angles, sketch):
    width = left_core.shape[3]
    local_sites = left_core.shape[1]
    local_rows = 2 * local_sites
    both = jnp.stack([left_core[0], right_core[0]], axis=1)
    both = lax.all_gather(both, "row", axis=0, tiled=True)
    sites = both.shape[0]
    left_matrix = both[:, 0].reshape(2 * sites, width)
    right_matrix = both[:, 1].reshape(sites, 2 * width)
    two_site = matmul(left_matrix, right_matrix)
    two_site = apply_gate(two_site, build_gate(gate_angles[0]))
    full_sketch = doubling_gather(sketch, "bond")
    ortho_basis = orthonormal(matmul(two_site, full_sketch))
    for repeat in range(ITERS):
        projected = inner_rows(two_site, ortho_basis)
        ortho_basis = orthonormal(matmul(two_site, projected))
    start = lax.axis_index("row") * local_sites
    my_columns = lax.dynamic_slice_in_dim(ortho_basis, start, local_sites, axis=1)
    carried = inner_rows(my_columns, two_site)
    incoming = from_behind(carried, "bond", 1)
    incoming_matrix = incoming.reshape(local_rows, width)
    next_block = matmul(incoming_matrix, ortho_basis.reshape(sites, 2 * width))
    return next_block[None]


def solution(mesh):
    return jax.shard_map(
        on_device,
        mesh=mesh,
        in_specs=(
            P("bond", "row", None, None),
            P("bond", "row", None, None),
            P("bond", None),
            P("bond", None),
        ),
        out_specs=P("bond", "row", None),
        check_vma=False,
    )
```

```python
import jax
import jax.numpy as jnp
import numpy as np
from jax import lax
from jax.experimental import pallas as pl
from jax.experimental.pallas import tpu as pltpu
from jax.sharding import PartitionSpec as P

ITERS = 2


HIGHEST = lax.Precision.HIGHEST
PLANES = ((0, 1), (2, 3), (0, 2), (1, 3), (0, 3), (1, 2))


def from_behind(value, axis, steps):
    count = lax.axis_size(axis)
    initial, last = (max(0, -steps), min(count, count - steps))
    return lax.ppermute(value, axis, [(source, source + steps) for source in range(initial, last)])


def rotation(first_axis, second_axis, cosine, sine_value):
    unit = np.eye(4, dtype=np.float32)
    diag_part = np.outer(unit[first_axis], unit[first_axis]) + np.outer(
        unit[second_axis], unit[second_axis]
    )
    skew_part = np.outer(unit[second_axis], unit[first_axis]) - np.outer(
        unit[first_axis], unit[second_axis]
    )
    rest_part = np.eye(4, dtype=np.float32) - diag_part
    return (
        jnp.asarray(rest_part)
        + cosine * jnp.asarray(diag_part)
        + sine_value * jnp.asarray(skew_part)
    )


def build_gate(angles):
    gate_matrix = jnp.eye(4, dtype=jnp.float32)
    for number, plane in enumerate(PLANES):
        rotated = rotation(plane[0], plane[1], jnp.cos(angles[number]), jnp.sin(angles[number]))
        gate_matrix = jnp.dot(
            rotated, gate_matrix, precision=HIGHEST, preferred_element_type=jnp.float32
        )
    return gate_matrix


def apply_gate(two_site, gate_matrix):
    width = two_site.shape[1] // 2
    blocks = two_site.reshape(two_site.shape[0] // 2, 2, 2, width)
    gate_parts = gate_matrix.reshape(2, 2, 2, 2)
    mixed_gate = sum(
        gate_parts[None, :, :, t, u, None] * blocks[:, None, None, t, u, :]
        for t in range(2)
        for u in range(2)
    )
    return mixed_gate.reshape(two_site.shape)


def matmul(left_side, right_side):
    return jnp.dot(left_side, right_side, precision=HIGHEST, preferred_element_type=jnp.float32)


def inner_rows(left_side, right_side):
    return lax.dot_general(
        left_side,
        right_side,
        (((0,), (0,)), ((), ())),
        precision=HIGHEST,
        preferred_element_type=jnp.float32,
    )


BLOCK = 128


def block_dot(left_side, right_side):
    return jnp.dot(left_side, right_side, precision=HIGHEST, preferred_element_type=jnp.float32)


def pick_pair(ref, base, offset, lanes):
    tile = ref[pl.ds(base, 8), lanes]
    sub = lax.broadcasted_iota(jnp.int32, tile.shape, 0)
    first = jnp.sum(jnp.where(sub == offset, tile, 0.0), axis=0, keepdims=True)
    second = jnp.sum(jnp.where(sub == offset + 1, tile, 0.0), axis=0, keepdims=True)
    return first, second


def lane_pick(row, lane, index):
    return jnp.sum(jnp.where(lane == index, row, 0.0), axis=1, keepdims=True)


def chol_inv_kernel(a_ref, w_ref, s_ref):
    n = a_ref.shape[0]
    nb = BLOCK
    blocks = n // nb
    s_ref[...] = a_ref[...]
    w_ref[...] = jnp.zeros((n, n), jnp.float32)
    eye_rows = lax.broadcasted_iota(jnp.int32, (nb, nb), 0)
    eye_cols = lax.broadcasted_iota(jnp.int32, (nb, nb), 1)
    eye = jnp.where(eye_rows == eye_cols, 1.0, 0.0).astype(jnp.float32)
    for p in range(blocks):
        r0 = p * nb
        diag = (slice(r0, r0 + nb), slice(r0, r0 + nb))
        w_ref[diag] = eye

        def step(t, carry):
            j = r0 + 2 * t
            base = pl.multiple_of(r0 + (t // 4) * 8, 8)
            offset = 2 * t - (t // 4) * 8
            lane = lax.broadcasted_iota(jnp.int32, (1, nb), 1) + r0
            row0, row1 = pick_pair(s_ref, base, offset, slice(r0, r0 + nb))
            a00 = lane_pick(row0, lane, j)
            a01 = lane_pick(row0, lane, j + 1)
            a11 = lane_pick(row1, lane, j + 1)
            inv0 = lax.rsqrt(a00)
            l10 = a01 * inv0
            inv1 = lax.rsqrt(a11 - l10 * l10)
            right0 = row0 * inv0
            right1 = (row1 - right0 * l10) * inv1
            later = lane > j + 1
            right0 = jnp.where(later, right0, 0.0)
            right1 = jnp.where(later, right1, 0.0)
            block = s_ref[diag]
            lane_d = lax.broadcasted_iota(jnp.int32, (nb, nb), 1) + r0
            col0 = jnp.sum(jnp.where(lane_d == j, block, 0.0), axis=1, keepdims=True)
            col1 = jnp.sum(jnp.where(lane_d == j + 1, block, 0.0), axis=1, keepdims=True)
            row_id = lax.broadcasted_iota(jnp.int32, (nb, 1), 0) + r0
            left0 = col0 * inv0
            left1 = (col1 - left0 * l10) * inv1
            below = row_id > j + 1
            down0 = jnp.where(below, left0, 0.0)
            down1 = jnp.where(below, left1, 0.0)
            updated = block - down0 * right0 - down1 * right1
            keep0 = jnp.where(row_id >= j, left0, 0.0)
            keep1 = jnp.where(row_id >= j + 1, left1, 0.0)
            s_ref[diag] = jnp.where(lane_d == j, keep0, jnp.where(lane_d == j + 1, keep1, updated))
            w0, w1 = pick_pair(w_ref, base, offset, slice(r0, r0 + nb))
            w0 = w0 * inv0
            w1 = (w1 - l10 * w0) * inv1
            w_block = w_ref[diag] - down0 * w0 - down1 * w1
            sub = lax.broadcasted_iota(jnp.int32, (nb, nb), 0) + r0
            w_ref[diag] = jnp.where(sub == j, w0, jnp.where(sub == j + 1, w1, w_block))
            return carry

        lax.fori_loop(0, nb // 2, step, 0, unroll=2)
        if p + 1 < blocks:
            panel = lax.dot_general(
                s_ref[r0 + nb:n, r0:r0 + nb], w_ref[diag], (((1,), (1,)), ((), ())),
                precision=HIGHEST, preferred_element_type=jnp.float32,
            )
            s_ref[r0 + nb:n, r0:r0 + nb] = panel
            s_ref[r0 + nb:n, r0 + nb:n] = s_ref[r0 + nb:n, r0 + nb:n] - lax.dot_general(
                panel, panel, (((1,), (1,)), ((), ())),
                precision=HIGHEST, preferred_element_type=jnp.float32,
            )
    for a in range(1, blocks):
        for b in range(a - 1, -1, -1):
            acc = jnp.zeros((nb, nb), jnp.float32)
            for k in range(b, a):
                acc = acc + block_dot(
                    s_ref[a * nb:(a + 1) * nb, k * nb:(k + 1) * nb],
                    w_ref[k * nb:(k + 1) * nb, b * nb:(b + 1) * nb],
                )
            w_ref[a * nb:(a + 1) * nb, b * nb:(b + 1) * nb] = -block_dot(
                w_ref[a * nb:(a + 1) * nb, a * nb:(a + 1) * nb], acc
            )


def chol_inv(gram):
    n = gram.shape[0]
    return pl.pallas_call(
        chol_inv_kernel,
        out_shape=jax.ShapeDtypeStruct((n, n), jnp.float32),
        in_specs=[pl.BlockSpec(memory_space=pltpu.VMEM)],
        out_specs=pl.BlockSpec(memory_space=pltpu.VMEM),
        scratch_shapes=[pltpu.VMEM((n, n), jnp.float32)],
    )(gram)

def orthonormal(sketched):
    gram_matrix = inner_rows(sketched, sketched)
    inverse_factor = chol_inv(gram_matrix)
    return lax.dot_general(
        sketched,
        inverse_factor,
        (((1,), (1,)), ((), ())),
        precision=HIGHEST,
        preferred_element_type=jnp.float32,
    )


def doubling_gather(block, axis):
    count = lax.axis_size(axis)
    index = lax.axis_index(axis)
    bits = count.bit_length() - 1
    gathered = block[None]
    for bit in reversed(range(bits)):
        mask = 1 << bit
        received = lax.ppermute(gathered, axis, [(source, source ^ mask) for source in range(count)])
        upper = (index & mask) != 0
        gathered = jnp.where(
            upper,
            jnp.stack([received, gathered]),
            jnp.stack([gathered, received]),
        )
    order = tuple(range(bits - 1, -1, -1)) + tuple(range(bits, gathered.ndim))
    gathered = jnp.transpose(gathered, order)
    return gathered.reshape((count * block.shape[0],) + block.shape[1:])


def on_device(left_core, right_core, gate_angles, sketch):
    width = left_core.shape[3]
    local_sites = left_core.shape[1]
    local_rows = 2 * local_sites
    both = jnp.stack([left_core[0], right_core[0]], axis=0)
    both = lax.all_gather(both, "row", axis=1, tiled=True)
    sites = both.shape[1]
    left_matrix = both[0].reshape(2 * sites, width)
    right_matrix = both[1].reshape(sites, 2 * width)
    two_site = matmul(left_matrix, right_matrix)
    two_site = apply_gate(two_site, build_gate(gate_angles[0]))
    full_sketch = doubling_gather(sketch, "bond")
    ortho_basis = orthonormal(matmul(two_site, full_sketch))
    for repeat in range(ITERS):
        projected = inner_rows(two_site, ortho_basis)
        ortho_basis = orthonormal(matmul(two_site, projected))
    start = lax.axis_index("row") * local_sites
    my_columns = lax.dynamic_slice_in_dim(ortho_basis, start, local_sites, axis=1)
    carried = inner_rows(my_columns, two_site)
    incoming = from_behind(carried, "bond", 1)
    incoming_matrix = incoming.reshape(local_rows, width)
    next_block = matmul(incoming_matrix, ortho_basis.reshape(sites, 2 * width))
    return next_block[None]


def solution(mesh):
    return jax.shard_map(
        on_device,
        mesh=mesh,
        in_specs=(
            P("bond", "row", None, None),
            P("bond", "row", None, None),
            P("bond", None),
            P("bond", None),
        ),
        out_specs=P("bond", "row", None),
        check_vma=False,
    )
```
